256 devices in a mesh: kv: 8 (over z), blk: 32 (over y, x, core).
Axes of the slice: x: 4, y: 4, z: 8, core: 2. Of those that a mesh axis runs over, the one named last changes fastest.
Arguments:
- embeds: bfloat16 [1, 256, 3072], P(None, None, 'blk'), may hold values from -40 to 40
- attn_norm: float32 [3072], P('blk'), may hold values from 0.25 to 1.75
- query_key_value_weight: bfloat16 [3072, 5120], P('blk', 'kv'), may hold values from -0.109375 to 0.109375
- w_out: bfloat16 [3072, 3072], P('kv', 'blk'), may hold values from -0.109375 to 0.109375
- mlp_norm: float32 [3072], P('blk'), may hold values from 0.25 to 1.75
- w_gate: bfloat16 [3072, 8192], P('blk', 'kv'), may hold values from -0.109375 to 0.109375
- w_up: bfloat16 [3072, 8192], P('blk', 'kv'), may hold values from -0.109375 to 0.109375
- w_down: bfloat16 [8192, 3072], P('kv', 'blk'), may hold values from -0.0625 to 0.0625
- prompt_key_slots: bfloat16 [256, 8, 128, 128], P('blk', 'kv'), may hold values from -210 to 210
- prompt_value_slots: bfloat16 [256, 8, 128, 128], P('blk', 'kv'), may hold values from -6 to 6
- generated_keys: bfloat16 [256, 8, 127, 128], P('blk', 'kv'), may hold values from -10 to 10
- generated_values: bfloat16 [256, 8, 127, 128], P('blk', 'kv'), may hold values from -6 to 6
- parents: int32 [1, 256], P(None, 'blk'), may hold values from 0 to 7
- prompt_length: int32 [32], replicated, may hold values from 1024 to 8192
- tenant_bounds: int32 [5], replicated, may hold values from 0 to 32, as said below
- slot_table: int32 [256], P('blk'), may hold values from 0 to 256, as said below
Outputs:
- hidden_out: float32 [1, 256, 3072], P(None, None, 'blk')
- keys_out: bfloat16 [256, 8, 128, 128], P('blk', 'kv')
- values_out: bfloat16 [256, 8, 128, 128], P('blk', 'kv')
The draws below stay inside these ranges and needn't reach their ends.
Inputs may be any that keep to these rules, and one draw needn't show every extreme that they name: parents[s, b] is the beam, among the 8 beams of b's request, whose cache beam b continues at step s. tenant_bounds[0] = 0 and tenant_bounds[4] = 32, strictly rising. `slot_table`: with L_t the largest prompt_length of tenant t's requests, every block j below ceil(L_t / 128) of every tenant t stands in exactly one slot as t * 64 + j, no other block stands anywhere, and 256 marks an empty slot.
All inputs are finite; a program needn't handle non-finite values.
Results may differ from the reference program's by a relative error of at most 0.012.
The reference program's roundings to bfloat16 on the way count: a program that leaves them out, or rounds other values in their place, can miss the bound.
Values may be sent and summed in bfloat16 or wider, within the bound.
No kernel may reach another device: no remote copies, remote signals or barrier semaphores. Data moves between devices by JAX's collectives and lax.ppermute only.
A program may use at most 64 MiB of HBM per device.

```python
import math
import jax
import jax.numpy as jnp
from jax import lax

MODEL_WIDTH = 3072
QUERY_HEADS = 24
KEY_VALUE_HEADS = 8
HEAD_WIDTH = 128
FF = 8192
GROUP_HEADS = 3
REQUEST_BEAMS = 8
TENANT_COUNT = 4
REQUEST_COUNT = 32
TOTAL_BEAMS = 256
PROMPT_POSITIONS = 8192
BLOCK_POSITIONS = 128
PROMPT_BLOCKS = 64
BLOCK_SLOTS = 256
EARLIER_TOKENS = 127
DECODE_STEPS = 1
GENERATED_LENGTH = 128


def layout_tables(key):
    random_subkeys = jax.random.split(jax.random.fold_in(key, 29), 4)
    cuts = jnp.sort(jax.random.permutation(random_subkeys[0], REQUEST_COUNT - 1)[:TENANT_COUNT - 1] + 1).astype(jnp.int32)
    bounds = jnp.concatenate([jnp.zeros((1,), jnp.int32), cuts, jnp.full((1,), REQUEST_COUNT, jnp.int32)])
    request_ids = jnp.arange(REQUEST_COUNT, dtype=jnp.int32)
    lengths = jax.random.randint(random_subkeys[1], (REQUEST_COUNT,), PROMPT_POSITIONS // 8, PROMPT_POSITIONS - BLOCK_POSITIONS + 1)
    picks = jax.random.permutation(random_subkeys[2], REQUEST_COUNT)
    lengths = jnp.where(request_ids == picks[0], PROMPT_POSITIONS, lengths)
    lengths = jnp.where(request_ids == picks[1], PROMPT_POSITIONS // 8, lengths).astype(jnp.int32)
    request_tenant = jnp.sum((request_ids[:, None] >= bounds[None, 1:TENANT_COUNT]).astype(jnp.int32), axis=1)
    longest = jnp.max(jnp.where(request_tenant[:, None] == jnp.arange(TENANT_COUNT, dtype=jnp.int32)[None, :], lengths[:, None], 0), axis=0)
    needed = (longest + BLOCK_POSITIONS - 1) // BLOCK_POSITIONS
    block_ids = jnp.arange(BLOCK_SLOTS, dtype=jnp.int32)
    valid = block_ids % PROMPT_BLOCKS < needed[block_ids // PROMPT_BLOCKS]
    order = jnp.argsort(1 - valid.astype(jnp.int32), stable=True)
    filled = jnp.sum(valid.astype(jnp.int32))
    entries = jnp.where(block_ids < filled, block_ids[order], BLOCK_SLOTS).astype(jnp.int32)
    places = jax.random.permutation(random_subkeys[3], BLOCK_SLOTS)
    table = jnp.zeros((BLOCK_SLOTS,), jnp.int32).at[places].set(entries)
    return (bounds, lengths, table)


def draw_tenant_bounds(key, part):
    return layout_tables(key)[0]


def draw_prompt_length(key, part):
    return layout_tables(key)[1]


def draw_slot_table(key, part):
    return layout_tables(key)[2]


def draw_embeds(key, part):
    random_subkeys = jax.random.split(jax.random.fold_in(key, 11), 4)
    row_scale = jnp.exp(jax.random.uniform(random_subkeys[0], (DECODE_STEPS, TOTAL_BEAMS, 1), jnp.float32, -0.8, 0.8))
    rough_scale = jnp.exp(jax.random.uniform(random_subkeys[1], (1, 1, MODEL_WIDTH), jnp.float32, -0.35, 0.35))
    column_frac = jnp.arange(MODEL_WIDTH, dtype=jnp.float32)[None, None, :] / (MODEL_WIDTH - 1.0) - 0.5
    ramp_scale = jnp.exp(column_frac * math.log(4.0))
    base_draw = jnp.clip(jax.random.normal(random_subkeys[3], (DECODE_STEPS, TOTAL_BEAMS, MODEL_WIDTH), jnp.float32), -4.0, 4.0)
    return (base_draw * row_scale * rough_scale * ramp_scale).astype(jnp.bfloat16)


def draw_prompt_key_slots(key, part):
    random_subkeys = jax.random.split(jax.random.fold_in(key, 13), 1)
    complete_shape = (BLOCK_SLOTS, KEY_VALUE_HEADS, BLOCK_POSITIONS, HEAD_WIDTH)
    result = jnp.clip(2.0 * jax.random.normal(random_subkeys[0], complete_shape, jnp.float32), -10.0, 10.0)
    return result.astype(jnp.bfloat16)


def with_ends(array, own_key, smallest, top_value):
    shape = array.shape
    place = [jax.random.randint(jax.random.fold_in(own_key, axis), (), 0, shape[axis]) for axis in range(len(shape))]
    array = array.at[tuple(place)].set(smallest)
    longest = shape.index(max(shape))
    place[longest] = (place[longest] + 1) % shape[longest]
    return array.at[tuple(place)].set(top_value)


def block_levels(own_key, extent, shards, least, top_value):
    level, own = 1.0, jax.random.fold_in(own_key, 6)
    for dim, shards_of in shards:
        draws = jnp.exp(jax.random.uniform(jax.random.fold_in(own, dim), (shards_of,), jnp.float32, least / len(shards), top_value / len(shards)))
        level = level * jnp.repeat(draws, extent[dim] // shards_of).reshape([-1 if axis == dim else 1 for axis in range(len(extent))])
    return level


def normal_values(key, dims, deviation, most, cuts=(), held_as=jnp.bfloat16):
    values = deviation * jax.random.normal(key, dims, jnp.float32)
    if cuts:
        values = values * block_levels(key, dims, cuts, -0.22, 0.18)
    return jnp.clip(values, -most, most).astype(held_as)


def setup_inputs(seed: int = 0) -> dict:
    keys = jax.random.split(jax.random.key(seed), 17)
    return {
        "embeds": draw_embeds(jax.random.fold_in(keys[16], 71), 0),
        "attn_norm": jnp.clip(1.0 + 0.15 * jax.random.normal(keys[1], (MODEL_WIDTH,), jnp.float32), 0.25, 1.75),
        "query_key_value_weight": normal_values(keys[2], (MODEL_WIDTH, KEY_VALUE_HEADS * (GROUP_HEADS + 2) * HEAD_WIDTH), MODEL_WIDTH ** -0.5, 0.109375, ((0, 32), (1, 8))),
        "w_out": normal_values(keys[3], (QUERY_HEADS * HEAD_WIDTH, MODEL_WIDTH), (QUERY_HEADS * HEAD_WIDTH) ** -0.5, 0.109375, ((0, 8), (1, 32))),
        "mlp_norm": jnp.clip(1.0 + 0.15 * jax.random.normal(keys[4], (MODEL_WIDTH,), jnp.float32), 0.25, 1.75),
        "w_gate": normal_values(keys[5], (MODEL_WIDTH, FF), MODEL_WIDTH ** -0.5, 0.109375, ((0, 32), (1, 8))),
        "w_up": normal_values(keys[6], (MODEL_WIDTH, FF), MODEL_WIDTH ** -0.5, 0.109375, ((0, 32), (1, 8))),
        "w_down": normal_values(keys[7], (FF, MODEL_WIDTH), FF ** -0.5, 0.0625, ((0, 8), (1, 32))),
        "prompt_key_slots": draw_prompt_key_slots(jax.random.fold_in(keys[16], 71), 0),
        "prompt_value_slots": normal_values(keys[9], (BLOCK_SLOTS, KEY_VALUE_HEADS, BLOCK_POSITIONS, HEAD_WIDTH), 1.0, 6.0, ((0, 32), (1, 8))),
        "generated_keys": normal_values(keys[10], (TOTAL_BEAMS, KEY_VALUE_HEADS, EARLIER_TOKENS, HEAD_WIDTH), 2.0, 10.0, ((0, 32), (1, 8))),
        "generated_values": normal_values(keys[11], (TOTAL_BEAMS, KEY_VALUE_HEADS, EARLIER_TOKENS, HEAD_WIDTH), 1.0, 6.0, ((0, 32), (1, 8))),
        "parents": with_ends(jax.random.randint(keys[12], (DECODE_STEPS, TOTAL_BEAMS), 0, REQUEST_BEAMS), jax.random.fold_in(keys[12], 1), 0, REQUEST_BEAMS - 1).astype(jnp.int32),
        "prompt_length": draw_prompt_length(jax.random.fold_in(keys[16], 71), 0),
        "tenant_bounds": draw_tenant_bounds(jax.random.fold_in(keys[16], 71), 0),
        "slot_table": draw_slot_table(jax.random.fold_in(keys[16], 71), 0),
    }


masked_score = -1e+30

def rotate(values, angles):
    half = values.shape[-1] // 2
    first = values[..., :half]
    second = values[..., half:]
    cosine = jnp.cos(angles)
    sine = jnp.sin(angles)
    return jnp.concatenate([first * cosine - second * sine, second * cosine + first * sine], axis=-1)

def angles_for(positions, head_size):
    half = head_size // 2
    freq = jnp.exp(jnp.arange(half, dtype=jnp.float32) * (-math.log(500000.0) / half))
    return positions.astype(jnp.float32)[:, None] * freq[None, :]

def reference(embeds, attn_norm, query_key_value_weight, w_out, mlp_norm, w_gate, w_up, w_down, prompt_key_slots, prompt_value_slots, generated_keys, generated_values, parents, prompt_length, tenant_bounds, slot_table):
    group_queries = QUERY_HEADS // KEY_VALUE_HEADS
    score_scale = 1.0 / math.sqrt(HEAD_WIDTH)
    request_ids = jnp.arange(REQUEST_COUNT, dtype=jnp.int32)
    request_tenant = lax.optimization_barrier(jnp.sum((request_ids[:, None] >= tenant_bounds[None, 1:TENANT_COUNT]).astype(jnp.int32), axis=1))
    placeholder_array = jnp.zeros((BLOCK_SLOTS + 1,), jnp.int32).at[slot_table].set(jnp.arange(BLOCK_SLOTS, dtype=jnp.int32))[:BLOCK_SLOTS]
    ordered_key_rows = prompt_key_slots[placeholder_array].reshape(TENANT_COUNT, PROMPT_BLOCKS, KEY_VALUE_HEADS, BLOCK_POSITIONS, HEAD_WIDTH).transpose(0, 2, 1, 3, 4).reshape(TENANT_COUNT, KEY_VALUE_HEADS, PROMPT_POSITIONS, HEAD_WIDTH)
    ordered_value_rows = prompt_value_slots[placeholder_array].reshape(TENANT_COUNT, PROMPT_BLOCKS, KEY_VALUE_HEADS, BLOCK_POSITIONS, HEAD_WIDTH).transpose(0, 2, 1, 3, 4).reshape(TENANT_COUNT, KEY_VALUE_HEADS, PROMPT_POSITIONS, HEAD_WIDTH)
    beam_req = jnp.arange(TOTAL_BEAMS, dtype=jnp.int32) // REQUEST_BEAMS
    length_beam = prompt_length[beam_req]
    trailing_zeros = jnp.zeros((TOTAL_BEAMS, KEY_VALUE_HEADS, DECODE_STEPS, HEAD_WIDTH), jnp.bfloat16)
    cached_key_rows = jnp.concatenate([generated_keys, trailing_zeros], axis=2)
    cached_value_rows = jnp.concatenate([generated_values, trailing_zeros], axis=2)
    key_pos = jnp.arange(PROMPT_POSITIONS, dtype=jnp.int32)
    gen_pos = jnp.arange(GENERATED_LENGTH, dtype=jnp.int32)
    outputs = []
    for step in range(DECODE_STEPS):
        residual = embeds[step].astype(jnp.float32)
        inverse = lax.rsqrt(lax.optimization_barrier(jnp.mean(residual * residual, axis=1)) + 1e-05)
        normed = (residual * attn_norm).astype(jnp.bfloat16)
        projected_rows = jnp.dot(normed, query_key_value_weight, preferred_element_type=jnp.float32) * inverse[:, None]
        projected_rows = projected_rows.reshape(TOTAL_BEAMS, KEY_VALUE_HEADS, group_queries + 2, HEAD_WIDTH)
        angles = angles_for(length_beam + EARLIER_TOKENS + step, HEAD_WIDTH)
        query_rows = rotate(projected_rows[:, :, :group_queries], angles[:, None, None, :]).astype(jnp.bfloat16)
        new_key = rotate(projected_rows[:, :, group_queries], angles[:, None, :]).astype(jnp.bfloat16)
        new_value = projected_rows[:, :, group_queries + 1].astype(jnp.bfloat16)
        parent_rows = beam_req * REQUEST_BEAMS + parents[step]
        cached_key_rows = cached_key_rows[parent_rows].at[:, :, EARLIER_TOKENS + step].set(new_key)
        cached_value_rows = cached_value_rows[parent_rows].at[:, :, EARLIER_TOKENS + step].set(new_value)

        def attend_heads(items):
            query, keys_gen, values_gen, length, tenant = items
            query_f = query.astype(jnp.float32)
            tenant_keys = ordered_key_rows[tenant].astype(jnp.float32)
            tenant_values = ordered_value_rows[tenant].astype(jnp.float32)
            prompt_scores = jnp.einsum('bkgd,knd->bkgn', query_f, tenant_keys) * score_scale
            gen_scores = jnp.einsum('bkgd,bknd->bkgn', query_f, keys_gen.astype(jnp.float32)) * score_scale
            scores = jnp.concatenate([prompt_scores, gen_scores], axis=3)
            mask = jnp.concatenate([key_pos < length, gen_pos <= EARLIER_TOKENS + step])[None, None, None, :]
            top_score = lax.optimization_barrier(jnp.max(jnp.where(mask, scores, masked_score), axis=3, keepdims=True))
            weights = jnp.where(mask, jnp.exp(scores - top_score), 0.0)
            total_mass = lax.optimization_barrier(jnp.sum(weights, axis=3, keepdims=True))
            rounded = lax.optimization_barrier(weights.astype(jnp.bfloat16)).astype(jnp.float32)
            summed = jnp.einsum('bkgn,knd->bkgd', rounded[..., :PROMPT_POSITIONS], tenant_values)
            summed = summed + jnp.einsum('bkgn,bknd->bkgd', rounded[..., PROMPT_POSITIONS:], values_gen.astype(jnp.float32))
            return (summed / total_mass).astype(jnp.bfloat16)
        attended_output = lax.map(attend_heads, (query_rows.reshape(REQUEST_COUNT, REQUEST_BEAMS, KEY_VALUE_HEADS, group_queries, HEAD_WIDTH), cached_key_rows.reshape(REQUEST_COUNT, REQUEST_BEAMS, KEY_VALUE_HEADS, GENERATED_LENGTH, HEAD_WIDTH), cached_value_rows.reshape(REQUEST_COUNT, REQUEST_BEAMS, KEY_VALUE_HEADS, GENERATED_LENGTH, HEAD_WIDTH), prompt_length, request_tenant))
        heads_out = attended_output.reshape(TOTAL_BEAMS, QUERY_HEADS * HEAD_WIDTH)
        after_attn = residual + jnp.dot(heads_out, w_out, preferred_element_type=jnp.float32)
        inverse2 = lax.rsqrt(lax.optimization_barrier(jnp.mean(after_attn * after_attn, axis=1)) + 1e-05)
        normed2 = (after_attn * mlp_norm).astype(jnp.bfloat16)
        gate = jnp.dot(normed2, w_gate, preferred_element_type=jnp.float32) * inverse2[:, None]
        upper = jnp.dot(normed2, w_up, preferred_element_type=jnp.float32) * inverse2[:, None]
        hidden = (jax.nn.silu(gate) * upper).astype(jnp.bfloat16)
        outputs.append(after_attn + jnp.dot(hidden, w_down, preferred_element_type=jnp.float32))
    return (jnp.stack(outputs), cached_key_rows, cached_value_rows)
```

```python
import math

import jax
import jax.numpy as jnp
from jax import lax
from jax.sharding import PartitionSpec as P

MODEL_WIDTH = 3072
QUERY_HEADS = 24
KEY_VALUE_HEADS = 8
HEAD_WIDTH = 128
REQUEST_BEAMS = 8
TENANT_COUNT = 4
BLOCK_POSITIONS = 128
PROMPT_BLOCKS = 64
EARLIER_TOKENS = 127
DECODE_STEPS = 1


masked_score = -1e30


def exchange(value, axis, bit):
    count = lax.axis_size(axis)
    return lax.ppermute(value, axis, [(i, i ^ (1 << bit)) for i in range(count)])


def butterfly_sum(value, axis):
    count = lax.axis_size(axis)
    if count & (count - 1):
        return lax.psum(value, axis)
    for bit in range(count.bit_length() - 1):
        value = value + exchange(value, axis, bit)
    return value


def scatter_sum(value, axis):
    count = lax.axis_size(axis)
    pieces = value.reshape((count, value.shape[0] // count) + value.shape[1:])
    return jnp.sum(lax.all_to_all(pieces, axis, 0, 0, tiled=False), axis=0)


def rotate(values, angles):
    half = values.shape[-1] // 2
    first = values[..., :half]
    second = values[..., half:]
    cosine = jnp.cos(angles)
    sine = jnp.sin(angles)
    return jnp.concatenate(
        [first * cosine - second * sine, second * cosine + first * sine], axis=-1
    )


def angles_for(positions, head_size):
    half = head_size // 2
    freq = jnp.exp(jnp.arange(half, dtype=jnp.float32) * (-math.log(500000.0) / half))
    return positions.astype(jnp.float32)[:, None] * freq[None, :]


def across_heads(partial_value):
    return butterfly_sum(partial_value, "kv")


def body(
    embeds,
    attn_norm,
    query_key_value_weight,
    w_out,
    mlp_norm,
    w_gate,
    w_up,
    w_down,
    prompt_key_slots,
    prompt_value_slots,
    generated_keys,
    generated_values,
    parents,
    prompt_length,
    tenant_bounds,
    slot_table,
):
    blocks = lax.axis_size("blk")
    my_index = lax.axis_index("blk")
    all_rows = embeds.shape[1]
    own_rows = all_rows // blocks
    heads_kv = prompt_key_slots.shape[1]
    slots_here = prompt_key_slots.shape[0]
    keys_here = slots_here * BLOCK_POSITIONS
    group_queries = QUERY_HEADS // KEY_VALUE_HEADS
    col_width = group_queries + 2
    score_scale = 1.0 / math.sqrt(HEAD_WIDTH)
    unit_count = w_gate.shape[1]
    beam_req = jnp.arange(all_rows, dtype=jnp.int32) // REQUEST_BEAMS
    tenant_beam = jnp.sum(
        (beam_req[:, None] >= tenant_bounds[None, 1:TENANT_COUNT]).astype(jnp.int32), axis=1
    )
    length_beam = jnp.repeat(prompt_length, REQUEST_BEAMS)
    slot_tenant = jnp.repeat(slot_table // PROMPT_BLOCKS, BLOCK_POSITIONS)
    slot_pos = jnp.repeat(slot_table % PROMPT_BLOCKS * BLOCK_POSITIONS, BLOCK_POSITIONS) + jnp.tile(
        jnp.arange(BLOCK_POSITIONS, dtype=jnp.int32), slots_here
    )
    visible = (tenant_beam[:, None] == slot_tenant[None, :]) & (
        slot_pos[None, :] < length_beam[:, None]
    )
    prompt_mask = visible[None, :, None, :]
    keys_flat = prompt_key_slots.transpose(1, 0, 2, 3).reshape(heads_kv, keys_here, HEAD_WIDTH)
    values_flat = prompt_value_slots.transpose(1, 0, 2, 3).reshape(heads_kv, keys_here, HEAD_WIDTH)
    local_beam = jnp.arange(own_rows, dtype=jnp.int32)
    base_rows = local_beam // REQUEST_BEAMS * REQUEST_BEAMS
    trailing_zeros = jnp.zeros((own_rows, heads_kv, DECODE_STEPS, HEAD_WIDTH), jnp.bfloat16)
    cached_key_rows = jnp.concatenate([generated_keys, trailing_zeros], axis=2)
    cached_value_rows = jnp.concatenate([generated_values, trailing_zeros], axis=2)
    gen_pos = jnp.arange(EARLIER_TOKENS + DECODE_STEPS, dtype=jnp.int32)
    w_both = jnp.concatenate([w_gate, w_up], axis=1)
    residual = embeds[0].astype(jnp.float32)
    squares = jnp.sum(residual * residual, axis=1)
    normed = (residual * attn_norm).astype(jnp.bfloat16)
    partial_value = jnp.dot(normed, query_key_value_weight, preferred_element_type=jnp.float32)
    own_value = scatter_sum(jnp.concatenate([partial_value, squares[:, None]], axis=1), "blk")
    inverse = lax.rsqrt(own_value[:, -1] / MODEL_WIDTH + 1e-05)
    own_proj = (own_value[:, :-1] * inverse[:, None]).reshape(own_rows, heads_kv, col_width, HEAD_WIDTH)
    own_length = lax.dynamic_slice_in_dim(length_beam, my_index * own_rows, own_rows, 0)
    own_angle = angles_for(own_length + EARLIER_TOKENS + 0, HEAD_WIDTH)
    own_queries = rotate(own_proj[:, :, :group_queries], own_angle[:, None, None, :]).astype(
        jnp.bfloat16
    )
    query_rows = lax.all_gather(own_queries, "blk", axis=0, tiled=True)
    new_key = rotate(own_proj[:, :, group_queries], own_angle[:, None, :]).astype(jnp.bfloat16)
    new_value = own_proj[:, :, group_queries + 1].astype(jnp.bfloat16)
    parent_rows = base_rows + parents[0]
    cached_key_rows = (
        jnp.take(cached_key_rows, parent_rows, axis=0).at[:, :, EARLIER_TOKENS].set(new_key)
    )
    cached_value_rows = (
        jnp.take(cached_value_rows, parent_rows, axis=0).at[:, :, EARLIER_TOKENS].set(new_value)
    )
    grouped = query_rows.transpose(1, 0, 2, 3).reshape(
        heads_kv, all_rows * group_queries, HEAD_WIDTH
    )
    scores = jnp.einsum("kqd,knd->kqn", grouped, keys_flat, preferred_element_type=jnp.float32)
    scores = scores.reshape(heads_kv, all_rows, group_queries, keys_here) * score_scale
    top_score = jnp.max(jnp.where(prompt_mask, scores, masked_score), axis=3)
    weights = jnp.where(prompt_mask, jnp.exp(scores - top_score[..., None]), 0.0)
    total_mass = jnp.sum(weights, axis=3)
    flat_weights = weights.reshape(heads_kv, all_rows * group_queries, keys_here).astype(
        jnp.bfloat16
    )
    summed = jnp.einsum(
        "kqn,knd->kqd", flat_weights, values_flat, preferred_element_type=jnp.float32
    )
    summed = summed.reshape(heads_kv, all_rows, group_queries, HEAD_WIDTH)
    packed = jnp.concatenate([summed, top_score[..., None], total_mass[..., None]], axis=3)
    packed = packed.transpose(1, 0, 2, 3).reshape(
        blocks, own_rows, heads_kv, group_queries, HEAD_WIDTH + 2
    )
    parts = lax.all_to_all(packed, "blk", 0, 0, tiled=False)
    part_top = parts[..., HEAD_WIDTH]
    prompt_top = jnp.max(part_top, axis=0)
    part_factor = jnp.exp(part_top - prompt_top[None])
    prompt_mass = jnp.sum(parts[..., HEAD_WIDTH + 1] * part_factor, axis=0)
    prompt_sum = jnp.sum(parts[..., :HEAD_WIDTH] * part_factor[..., None], axis=0)
    prompt_top = prompt_top.transpose(1, 0, 2)
    prompt_mass = prompt_mass.transpose(1, 0, 2)
    prompt_sum = prompt_sum.transpose(1, 0, 2, 3)
    gen_scores = (
        jnp.einsum(
            "bkgd,bknd->kbgn", own_queries, cached_key_rows, preferred_element_type=jnp.float32
        )
        * score_scale
    )
    live = (gen_pos <= EARLIER_TOKENS)[None, None, None, :]
    gen_top = jnp.max(jnp.where(live, gen_scores, masked_score), axis=3)
    best = jnp.maximum(prompt_top, gen_top)
    gen_weights = jnp.where(live, jnp.exp(gen_scores - best[..., None]), 0.0)
    shift = jnp.exp(prompt_top - best)
    full_mass = prompt_mass * shift + jnp.sum(gen_weights, axis=3)
    gen_sum = jnp.einsum(
        "kbgn,bknd->kbgd",
        gen_weights.astype(jnp.bfloat16),
        cached_value_rows,
        preferred_element_type=jnp.float32,
    )
    attended_output = (prompt_sum * shift[..., None] + gen_sum) / full_mass[..., None]
    heads_out = (
        attended_output.transpose(1, 0, 2, 3)
        .reshape(own_rows, heads_kv * group_queries * HEAD_WIDTH)
        .astype(jnp.bfloat16)
    )
    head_part = jnp.dot(
        lax.all_gather(heads_out, "blk", axis=0, tiled=True),
        w_out,
        preferred_element_type=jnp.float32,
    )
    after_attn = residual + across_heads(head_part)
    squares2 = jnp.sum(after_attn * after_attn, axis=1)
    normed2 = (after_attn * mlp_norm).astype(jnp.bfloat16)
    mixed = scatter_sum(
        jnp.concatenate(
            [jnp.dot(normed2, w_both, preferred_element_type=jnp.float32), squares2[:, None]],
            axis=1,
        ),
        "blk",
    )
    own_inverse = lax.rsqrt(mixed[:, -1] / MODEL_WIDTH + 1e-05)
    gate = mixed[:, :unit_count] * own_inverse[:, None]
    upper = mixed[:, unit_count : 2 * unit_count] * own_inverse[:, None]
    hidden = (jax.nn.silu(gate) * upper).astype(jnp.bfloat16)
    ff_part = jnp.dot(
        lax.all_gather(hidden, "blk", axis=0, tiled=True),
        w_down,
        preferred_element_type=jnp.float32,
    )
    outputs = [after_attn + across_heads(ff_part)]
    return (jnp.stack(outputs), cached_key_rows, cached_value_rows)


def solution(mesh):
    in_specs = (
        P(None, None, "blk"),
        P("blk"),
        P("blk", "kv"),
        P("kv", "blk"),
        P("blk"),
        P("blk", "kv"),
        P("blk", "kv"),
        P("kv", "blk"),
        P("blk", "kv", None, None),
        P("blk", "kv", None, None),
        P("blk", "kv", None, None),
        P("blk", "kv", None, None),
        P(None, "blk"),
        P(),
        P(),
        P("blk"),
    )
    out_specs = (P(None, None, "blk"), P("blk", "kv", None, None), P("blk", "kv", None, None))
    return jax.shard_map(body, mesh=mesh, in_specs=in_specs, out_specs=out_specs, check_vma=False)
```

```python
import math

import jax
import jax.numpy as jnp
from jax import lax
from jax.sharding import PartitionSpec as P

MODEL_WIDTH = 3072
QUERY_HEADS = 24
KEY_VALUE_HEADS = 8
HEAD_WIDTH = 128
REQUEST_BEAMS = 8
TENANT_COUNT = 4
BLOCK_POSITIONS = 128
PROMPT_BLOCKS = 64
EARLIER_TOKENS = 127
DECODE_STEPS = 1


masked_score = -1e30


def exchange(value, axis, bit):
    count = lax.axis_size(axis)
    return lax.ppermute(value, axis, [(i, i ^ (1 << bit)) for i in range(count)])


def butterfly_sum(value, axis):
    count = lax.axis_size(axis)
    if count & (count - 1):
        return lax.psum(value, axis)
    for bit in range(count.bit_length() - 1):
        value = value + exchange(value, axis, bit)
    return value


def scatter_sum(value, axis):
    count = lax.axis_size(axis)
    pieces = value.reshape((count, value.shape[0] // count) + value.shape[1:])
    return jnp.sum(lax.all_to_all(pieces, axis, 0, 0, tiled=False), axis=0)


def gather_rows(value, axis):
    count = lax.axis_size(axis)
    flat = jnp.broadcast_to(value.reshape(1, -1), (count, value.size))
    gathered = lax.all_to_all(flat, axis, 0, 0, tiled=False)
    return gathered.reshape((count * value.shape[0],) + value.shape[1:])


def rotate(values, angles):
    half = values.shape[-1] // 2
    first = values[..., :half]
    second = values[..., half:]
    cosine = jnp.cos(angles)
    sine = jnp.sin(angles)
    return jnp.concatenate(
        [first * cosine - second * sine, second * cosine + first * sine], axis=-1
    )


def angles_for(positions, head_size):
    half = head_size // 2
    freq = jnp.exp(jnp.arange(half, dtype=jnp.float32) * (-math.log(500000.0) / half))
    return positions.astype(jnp.float32)[:, None] * freq[None, :]


def across_heads(partial_value):
    return butterfly_sum(partial_value, "kv")


def body(
    embeds,
    attn_norm,
    query_key_value_weight,
    w_out,
    mlp_norm,
    w_gate,
    w_up,
    w_down,
    prompt_key_slots,
    prompt_value_slots,
    generated_keys,
    generated_values,
    parents,
    prompt_length,
    tenant_bounds,
    slot_table,
):
    blocks = lax.axis_size("blk")
    my_index = lax.axis_index("blk")
    all_rows = embeds.shape[1]
    own_rows = all_rows // blocks
    heads_kv = prompt_key_slots.shape[1]
    slots_here = prompt_key_slots.shape[0]
    keys_here = slots_here * BLOCK_POSITIONS
    group_queries = QUERY_HEADS // KEY_VALUE_HEADS
    col_width = group_queries + 2
    score_scale = 1.0 / math.sqrt(HEAD_WIDTH)
    unit_count = w_gate.shape[1]
    beam_req = jnp.arange(all_rows, dtype=jnp.int32) // REQUEST_BEAMS
    tenant_beam = jnp.sum(
        (beam_req[:, None] >= tenant_bounds[None, 1:TENANT_COUNT]).astype(jnp.int32), axis=1
    )
    length_beam = jnp.repeat(prompt_length, REQUEST_BEAMS)
    slot_tenant = jnp.repeat(slot_table // PROMPT_BLOCKS, BLOCK_POSITIONS)
    slot_pos = jnp.repeat(slot_table % PROMPT_BLOCKS * BLOCK_POSITIONS, BLOCK_POSITIONS) + jnp.tile(
        jnp.arange(BLOCK_POSITIONS, dtype=jnp.int32), slots_here
    )
    visible = (tenant_beam[:, None] == slot_tenant[None, :]) & (
        slot_pos[None, :] < length_beam[:, None]
    )
    prompt_mask = visible[None, :, None, :]
    keys_flat = prompt_key_slots.transpose(1, 0, 2, 3).reshape(heads_kv, keys_here, HEAD_WIDTH)
    values_flat = prompt_value_slots.transpose(1, 0, 2, 3).reshape(heads_kv, keys_here, HEAD_WIDTH)
    local_beam = jnp.arange(own_rows, dtype=jnp.int32)
    base_rows = local_beam // REQUEST_BEAMS * REQUEST_BEAMS
    trailing_zeros = jnp.zeros((own_rows, heads_kv, DECODE_STEPS, HEAD_WIDTH), jnp.bfloat16)
    cached_key_rows = jnp.concatenate([generated_keys, trailing_zeros], axis=2)
    cached_value_rows = jnp.concatenate([generated_values, trailing_zeros], axis=2)
    gen_pos = jnp.arange(EARLIER_TOKENS + DECODE_STEPS, dtype=jnp.int32)
    w_both = jnp.concatenate([w_gate, w_up], axis=1)
    residual = embeds[0].astype(jnp.float32)
    squares = jnp.sum(residual * residual, axis=1)
    normed = (residual * attn_norm).astype(jnp.bfloat16)
    partial_value = jnp.dot(normed, query_key_value_weight, preferred_element_type=jnp.float32)
    own_value = scatter_sum(jnp.concatenate([partial_value, squares[:, None]], axis=1), "blk")
    inverse = lax.rsqrt(own_value[:, -1] / MODEL_WIDTH + 1e-05)
    own_proj = (own_value[:, :-1] * inverse[:, None]).reshape(own_rows, heads_kv, col_width, HEAD_WIDTH)
    own_length = lax.dynamic_slice_in_dim(length_beam, my_index * own_rows, own_rows, 0)
    own_angle = angles_for(own_length + EARLIER_TOKENS + 0, HEAD_WIDTH)
    own_queries = rotate(own_proj[:, :, :group_queries], own_angle[:, None, None, :]).astype(
        jnp.bfloat16
    )
    query_rows = gather_rows(own_queries, "blk")
    new_key = rotate(own_proj[:, :, group_queries], own_angle[:, None, :]).astype(jnp.bfloat16)
    new_value = own_proj[:, :, group_queries + 1].astype(jnp.bfloat16)
    parent_rows = base_rows + parents[0]
    cached_key_rows = (
        jnp.take(cached_key_rows, parent_rows, axis=0).at[:, :, EARLIER_TOKENS].set(new_key)
    )
    cached_value_rows = (
        jnp.take(cached_value_rows, parent_rows, axis=0).at[:, :, EARLIER_TOKENS].set(new_value)
    )
    grouped = query_rows.transpose(1, 0, 2, 3).reshape(
        heads_kv, all_rows * group_queries, HEAD_WIDTH
    )
    scores = jnp.einsum("kqd,knd->kqn", grouped, keys_flat, preferred_element_type=jnp.float32)
    scores = scores.reshape(heads_kv, all_rows, group_queries, keys_here) * score_scale
    top_score = jnp.max(jnp.where(prompt_mask, scores, masked_score), axis=3)
    weights = jnp.where(prompt_mask, jnp.exp(scores - top_score[..., None]), 0.0)
    total_mass = jnp.sum(weights, axis=3)
    flat_weights = weights.reshape(heads_kv, all_rows * group_queries, keys_here).astype(
        jnp.bfloat16
    )
    summed = jnp.einsum(
        "kqn,knd->kqd", flat_weights, values_flat, preferred_element_type=jnp.float32
    )
    summed = summed.reshape(heads_kv, all_rows, group_queries, HEAD_WIDTH)
    packed = jnp.concatenate([summed, top_score[..., None], total_mass[..., None]], axis=3)
    packed = packed.transpose(1, 0, 2, 3).reshape(blocks, -1)
    parts = lax.all_to_all(packed, "blk", 0, 0, tiled=False).reshape(
        blocks, own_rows, heads_kv, group_queries, HEAD_WIDTH + 2
    )
    part_top = parts[..., HEAD_WIDTH]
    prompt_top = jnp.max(part_top, axis=0)
    part_factor = jnp.exp(part_top - prompt_top[None])
    prompt_mass = jnp.sum(parts[..., HEAD_WIDTH + 1] * part_factor, axis=0)
    prompt_sum = jnp.sum(parts[..., :HEAD_WIDTH] * part_factor[..., None], axis=0)
    prompt_top = prompt_top.transpose(1, 0, 2)
    prompt_mass = prompt_mass.transpose(1, 0, 2)
    prompt_sum = prompt_sum.transpose(1, 0, 2, 3)
    gen_scores = (
        jnp.einsum(
            "bkgd,bknd->kbgn", own_queries, cached_key_rows, preferred_element_type=jnp.float32
        )
        * score_scale
    )
    live = (gen_pos <= EARLIER_TOKENS)[None, None, None, :]
    gen_top = jnp.max(jnp.where(live, gen_scores, masked_score), axis=3)
    best = jnp.maximum(prompt_top, gen_top)
    gen_weights = jnp.where(live, jnp.exp(gen_scores - best[..., None]), 0.0)
    shift = jnp.exp(prompt_top - best)
    full_mass = prompt_mass * shift + jnp.sum(gen_weights, axis=3)
    gen_sum = jnp.einsum(
        "kbgn,bknd->kbgd",
        gen_weights.astype(jnp.bfloat16),
        cached_value_rows,
        preferred_element_type=jnp.float32,
    )
    attended_output = (prompt_sum * shift[..., None] + gen_sum) / full_mass[..., None]
    heads_out = (
        attended_output.transpose(1, 0, 2, 3)
        .reshape(own_rows, heads_kv * group_queries * HEAD_WIDTH)
        .astype(jnp.bfloat16)
    )
    head_part = jnp.dot(
        gather_rows(heads_out, "blk"),
        w_out,
        preferred_element_type=jnp.float32,
    )
    after_attn = residual + across_heads(head_part)
    squares2 = jnp.sum(after_attn * after_attn, axis=1)
    normed2 = (after_attn * mlp_norm).astype(jnp.bfloat16)
    mixed = scatter_sum(
        jnp.concatenate(
            [jnp.dot(normed2, w_both, preferred_element_type=jnp.float32), squares2[:, None]],
            axis=1,
        ),
        "blk",
    )
    own_inverse = lax.rsqrt(mixed[:, -1] / MODEL_WIDTH + 1e-05)
    gate = mixed[:, :unit_count] * own_inverse[:, None]
    upper = mixed[:, unit_count : 2 * unit_count] * own_inverse[:, None]
    hidden = (jax.nn.silu(gate) * upper).astype(jnp.bfloat16)
    ff_part = jnp.dot(
        gather_rows(hidden, "blk"),
        w_down,
        preferred_element_type=jnp.float32,
    )
    outputs = [after_attn + across_heads(ff_part)]
    return (jnp.stack(outputs), cached_key_rows, cached_value_rows)


def solution(mesh):
    in_specs = (
        P(None, None, "blk"),
        P("blk"),
        P("blk", "kv"),
        P("kv", "blk"),
        P("blk"),
        P("blk", "kv"),
        P("blk", "kv"),
        P("kv", "blk"),
        P("blk", "kv", None, None),
        P("blk", "kv", None, None),
        P("blk", "kv", None, None),
        P("blk", "kv", None, None),
        P(None, "blk"),
        P(),
        P(),
        P("blk"),
    )
    out_specs = (P(None, None, "blk"), P("blk", "kv", None, None), P("blk", "kv", None, None))
    return jax.shard_map(body, mesh=mesh, in_specs=in_specs, out_specs=out_specs, check_vma=False)
```

```python
import math

import jax
import jax.numpy as jnp
from jax import lax
from jax.sharding import PartitionSpec as P

MODEL_WIDTH = 3072
QUERY_HEADS = 24
KEY_VALUE_HEADS = 8
HEAD_WIDTH = 128
REQUEST_BEAMS = 8
TENANT_COUNT = 4
BLOCK_POSITIONS = 128
PROMPT_BLOCKS = 64
EARLIER_TOKENS = 127
DECODE_STEPS = 1


masked_score = -1e30


def exchange(value, axis, bit):
    count = lax.axis_size(axis)
    return lax.ppermute(value, axis, [(i, i ^ (1 << bit)) for i in range(count)])


def butterfly_sum(value, axis):
    count = lax.axis_size(axis)
    if count & (count - 1):
        return lax.psum(value, axis)
    for bit in range(count.bit_length() - 1):
        value = value + exchange(value, axis, bit)
    return value


def scatter_sum(value, axis, sum_type=None):
    count = lax.axis_size(axis)
    pieces = value.reshape((count, value.shape[0] // count) + value.shape[1:])
    return jnp.sum(lax.all_to_all(pieces, axis, 0, 0, tiled=False).astype(sum_type), axis=0)


def gather_rows(value, axis):
    count = lax.axis_size(axis)
    flat = jnp.broadcast_to(value.reshape(1, -1), (count, value.size))
    gathered = lax.all_to_all(flat, axis, 0, 0, tiled=False)
    return gathered.reshape((count * value.shape[0],) + value.shape[1:])


def rotate(values, angles):
    half = values.shape[-1] // 2
    first = values[..., :half]
    second = values[..., half:]
    cosine = jnp.cos(angles)
    sine = jnp.sin(angles)
    return jnp.concatenate(
        [first * cosine - second * sine, second * cosine + first * sine], axis=-1
    )


def angles_for(positions, head_size):
    half = head_size // 2
    freq = jnp.exp(jnp.arange(half, dtype=jnp.float32) * (-math.log(500000.0) / half))
    return positions.astype(jnp.float32)[:, None] * freq[None, :]


def across_heads(partial_value):
    return butterfly_sum(partial_value, "kv")


def body(
    embeds,
    attn_norm,
    query_key_value_weight,
    w_out,
    mlp_norm,
    w_gate,
    w_up,
    w_down,
    prompt_key_slots,
    prompt_value_slots,
    generated_keys,
    generated_values,
    parents,
    prompt_length,
    tenant_bounds,
    slot_table,
):
    blocks = lax.axis_size("blk")
    my_index = lax.axis_index("blk")
    all_rows = embeds.shape[1]
    own_rows = all_rows // blocks
    heads_kv = prompt_key_slots.shape[1]
    slots_here = prompt_key_slots.shape[0]
    keys_here = slots_here * BLOCK_POSITIONS
    group_queries = QUERY_HEADS // KEY_VALUE_HEADS
    col_width = group_queries + 2
    score_scale = 1.0 / math.sqrt(HEAD_WIDTH)
    unit_count = w_gate.shape[1]
    beam_req = jnp.arange(all_rows, dtype=jnp.int32) // REQUEST_BEAMS
    tenant_beam = jnp.sum(
        (beam_req[:, None] >= tenant_bounds[None, 1:TENANT_COUNT]).astype(jnp.int32), axis=1
    )
    length_beam = jnp.repeat(prompt_length, REQUEST_BEAMS)
    slot_tenant = jnp.repeat(slot_table // PROMPT_BLOCKS, BLOCK_POSITIONS)
    slot_pos = jnp.repeat(slot_table % PROMPT_BLOCKS * BLOCK_POSITIONS, BLOCK_POSITIONS) + jnp.tile(
        jnp.arange(BLOCK_POSITIONS, dtype=jnp.int32), slots_here
    )
    visible = (tenant_beam[:, None] == slot_tenant[None, :]) & (
        slot_pos[None, :] < length_beam[:, None]
    )
    prompt_mask = visible[None, :, None, :]
    keys_flat = prompt_key_slots.transpose(1, 0, 2, 3).reshape(heads_kv, keys_here, HEAD_WIDTH)
    values_flat = prompt_value_slots.transpose(1, 0, 2, 3).reshape(heads_kv, keys_here, HEAD_WIDTH)
    local_beam = jnp.arange(own_rows, dtype=jnp.int32)
    base_rows = local_beam // REQUEST_BEAMS * REQUEST_BEAMS
    trailing_zeros = jnp.zeros((own_rows, heads_kv, DECODE_STEPS, HEAD_WIDTH), jnp.bfloat16)
    cached_key_rows = jnp.concatenate([generated_keys, trailing_zeros], axis=2)
    cached_value_rows = jnp.concatenate([generated_values, trailing_zeros], axis=2)
    gen_pos = jnp.arange(EARLIER_TOKENS + DECODE_STEPS, dtype=jnp.int32)
    w_both = jnp.concatenate([w_gate, w_up], axis=1)
    residual = embeds[0].astype(jnp.float32)
    squares = jnp.sum(residual * residual, axis=1)
    normed = (residual * attn_norm).astype(jnp.bfloat16)
    partial_value = jnp.dot(normed, query_key_value_weight, preferred_element_type=jnp.float32)
    own_value = scatter_sum(jnp.concatenate([partial_value, squares[:, None]], axis=1), "blk")
    inverse = lax.rsqrt(own_value[:, -1] / MODEL_WIDTH + 1e-05)
    own_proj = (own_value[:, :-1] * inverse[:, None]).reshape(own_rows, heads_kv, col_width, HEAD_WIDTH)
    own_length = lax.dynamic_slice_in_dim(length_beam, my_index * own_rows, own_rows, 0)
    own_angle = angles_for(own_length + EARLIER_TOKENS + 0, HEAD_WIDTH)
    own_queries = rotate(own_proj[:, :, :group_queries], own_angle[:, None, None, :]).astype(
        jnp.bfloat16
    )
    query_rows = gather_rows(own_queries, "blk")
    new_key = rotate(own_proj[:, :, group_queries], own_angle[:, None, :]).astype(jnp.bfloat16)
    new_value = own_proj[:, :, group_queries + 1].astype(jnp.bfloat16)
    parent_rows = base_rows + parents[0]
    cached_key_rows = (
        jnp.take(cached_key_rows, parent_rows, axis=0).at[:, :, EARLIER_TOKENS].set(new_key)
    )
    cached_value_rows = (
        jnp.take(cached_value_rows, parent_rows, axis=0).at[:, :, EARLIER_TOKENS].set(new_value)
    )
    grouped = query_rows.transpose(1, 0, 2, 3).reshape(
        heads_kv, all_rows * group_queries, HEAD_WIDTH
    )
    scores = jnp.einsum("kqd,knd->kqn", grouped, keys_flat, preferred_element_type=jnp.float32)
    scores = scores.reshape(heads_kv, all_rows, group_queries, keys_here) * score_scale
    top_score = jnp.max(jnp.where(prompt_mask, scores, masked_score), axis=3)
    weights = jnp.where(prompt_mask, jnp.exp(scores - top_score[..., None]), 0.0)
    total_mass = jnp.sum(weights, axis=3)
    flat_weights = weights.reshape(heads_kv, all_rows * group_queries, keys_here).astype(
        jnp.bfloat16
    )
    summed = jnp.einsum(
        "kqn,knd->kqd", flat_weights, values_flat, preferred_element_type=jnp.float32
    )
    summed = summed.reshape(heads_kv, all_rows, group_queries, HEAD_WIDTH)
    packed = jnp.concatenate([summed, top_score[..., None], total_mass[..., None]], axis=3)
    packed = packed.transpose(1, 0, 2, 3).reshape(blocks, -1)
    parts = lax.all_to_all(packed, "blk", 0, 0, tiled=False).reshape(
        blocks, own_rows, heads_kv, group_queries, HEAD_WIDTH + 2
    )
    part_top = parts[..., HEAD_WIDTH]
    prompt_top = jnp.max(part_top, axis=0)
    part_factor = jnp.exp(part_top - prompt_top[None])
    prompt_mass = jnp.sum(parts[..., HEAD_WIDTH + 1] * part_factor, axis=0)
    prompt_sum = jnp.sum(parts[..., :HEAD_WIDTH] * part_factor[..., None], axis=0)
    prompt_top = prompt_top.transpose(1, 0, 2)
    prompt_mass = prompt_mass.transpose(1, 0, 2)
    prompt_sum = prompt_sum.transpose(1, 0, 2, 3)
    gen_scores = (
        jnp.einsum(
            "bkgd,bknd->kbgn", own_queries, cached_key_rows, preferred_element_type=jnp.float32
        )
        * score_scale
    )
    live = (gen_pos <= EARLIER_TOKENS)[None, None, None, :]
    gen_top = jnp.max(jnp.where(live, gen_scores, masked_score), axis=3)
    best = jnp.maximum(prompt_top, gen_top)
    gen_weights = jnp.where(live, jnp.exp(gen_scores - best[..., None]), 0.0)
    shift = jnp.exp(prompt_top - best)
    full_mass = prompt_mass * shift + jnp.sum(gen_weights, axis=3)
    gen_sum = jnp.einsum(
        "kbgn,bknd->kbgd",
        gen_weights.astype(jnp.bfloat16),
        cached_value_rows,
        preferred_element_type=jnp.float32,
    )
    attended_output = (prompt_sum * shift[..., None] + gen_sum) / full_mass[..., None]
    heads_out = (
        attended_output.transpose(1, 0, 2, 3)
        .reshape(own_rows, heads_kv * group_queries * HEAD_WIDTH)
        .astype(jnp.bfloat16)
    )
    head_part = jnp.dot(
        gather_rows(heads_out, "blk"),
        w_out,
        preferred_element_type=jnp.float32,
    )
    after_attn = residual + across_heads(head_part)
    squares2 = jnp.sum(after_attn * after_attn, axis=1)
    normed2 = (after_attn * mlp_norm).astype(jnp.bfloat16)
    squares2_high = squares2.astype(jnp.bfloat16)
    squares2_low = (squares2 - squares2_high.astype(jnp.float32)).astype(jnp.bfloat16)
    mixed = scatter_sum(
        jnp.concatenate(
            [
                jnp.dot(normed2, w_both, preferred_element_type=jnp.float32).astype(jnp.bfloat16),
                squares2_high[:, None],
                squares2_low[:, None],
            ],
            axis=1,
        ),
        "blk",
        jnp.float32,
    )
    own_inverse = lax.rsqrt((mixed[:, -2] + mixed[:, -1]) / MODEL_WIDTH + 1e-05)
    gate = mixed[:, :unit_count] * own_inverse[:, None]
    upper = mixed[:, unit_count : 2 * unit_count] * own_inverse[:, None]
    hidden = (jax.nn.silu(gate) * upper).astype(jnp.bfloat16)
    ff_part = jnp.dot(
        gather_rows(hidden, "blk"),
        w_down,
        preferred_element_type=jnp.float32,
    )
    outputs = [after_attn + across_heads(ff_part)]
    return (jnp.stack(outputs), cached_key_rows, cached_value_rows)


def solution(mesh):
    in_specs = (
        P(None, None, "blk"),
        P("blk"),
        P("blk", "kv"),
        P("kv", "blk"),
        P("blk"),
        P("blk", "kv"),
        P("blk", "kv"),
        P("kv", "blk"),
        P("blk", "kv", None, None),
        P("blk", "kv", None, None),
        P("blk", "kv", None, None),
        P("blk", "kv", None, None),
        P(None, "blk"),
        P(),
        P(),
        P("blk"),
    )
    out_specs = (P(None, None, "blk"), P("blk", "kv", None, None), P("blk", "kv", None, None))
    return jax.shard_map(body, mesh=mesh, in_specs=in_specs, out_specs=out_specs, check_vma=False)
```

```python
import math

import jax
import jax.numpy as jnp
from jax import lax
from jax.sharding import PartitionSpec as P

MODEL_WIDTH = 3072
QUERY_HEADS = 24
KEY_VALUE_HEADS = 8
HEAD_WIDTH = 128
REQUEST_BEAMS = 8
TENANT_COUNT = 4
BLOCK_POSITIONS = 128
PROMPT_BLOCKS = 64
EARLIER_TOKENS = 127
DECODE_STEPS = 1


masked_score = -1e30


def exchange(value, axis, bit):
    count = lax.axis_size(axis)
    return lax.ppermute(value, axis, [(i, i ^ (1 << bit)) for i in range(count)])


def butterfly_sum(value, axis):
    count = lax.axis_size(axis)
    if count & (count - 1):
        return lax.psum(value, axis)
    for bit in range(count.bit_length() - 1):
        value = value + exchange(value, axis, bit)
    return value


def scatter_sum(value, axis, sum_type=None):
    count = lax.axis_size(axis)
    pieces = value.reshape((count, value.shape[0] // count) + value.shape[1:])
    return jnp.sum(lax.all_to_all(pieces, axis, 0, 0, tiled=False).astype(sum_type), axis=0)


def scatter_sum_flat(value, axis):
    count = lax.axis_size(axis)
    piece_shape = (value.shape[0] // count,) + value.shape[1:]
    pieces = value.reshape(count, -1)
    return jnp.sum(lax.all_to_all(pieces, axis, 0, 0, tiled=False), axis=0).reshape(piece_shape)


def gather_rows(value, axis):
    count = lax.axis_size(axis)
    copies = jnp.broadcast_to(value[None], (count,) + value.shape)
    gathered = lax.all_to_all(copies, axis, 0, 0, tiled=False)
    return gathered.reshape((count * value.shape[0],) + value.shape[1:])


def rotate(values, angles):
    half = values.shape[-1] // 2
    first = values[..., :half]
    second = values[..., half:]
    cosine = jnp.cos(angles)
    sine = jnp.sin(angles)
    return jnp.concatenate(
        [first * cosine - second * sine, second * cosine + first * sine], axis=-1
    )


def angles_for(positions, head_size):
    half = head_size // 2
    freq = jnp.exp(jnp.arange(half, dtype=jnp.float32) * (-math.log(500000.0) / half))
    return positions.astype(jnp.float32)[:, None] * freq[None, :]


def across_heads(partial_value):
    return butterfly_sum(partial_value, "kv")


def body(
    embeds,
    attn_norm,
    query_key_value_weight,
    w_out,
    mlp_norm,
    w_gate,
    w_up,
    w_down,
    prompt_key_slots,
    prompt_value_slots,
    generated_keys,
    generated_values,
    parents,
    prompt_length,
    tenant_bounds,
    slot_table,
):
    blocks = lax.axis_size("blk")
    my_index = lax.axis_index("blk")
    all_rows = embeds.shape[1]
    own_rows = all_rows // blocks
    heads_kv = prompt_key_slots.shape[1]
    slots_here = prompt_key_slots.shape[0]
    keys_here = slots_here * BLOCK_POSITIONS
    group_queries = QUERY_HEADS // KEY_VALUE_HEADS
    col_width = group_queries + 2
    score_scale = 1.0 / math.sqrt(HEAD_WIDTH)
    unit_count = w_gate.shape[1]
    beam_req = jnp.arange(all_rows, dtype=jnp.int32) // REQUEST_BEAMS
    tenant_beam = jnp.sum(
        (beam_req[:, None] >= tenant_bounds[None, 1:TENANT_COUNT]).astype(jnp.int32), axis=1
    )
    length_beam = jnp.repeat(prompt_length, REQUEST_BEAMS)
    slot_tenant = jnp.repeat(slot_table // PROMPT_BLOCKS, BLOCK_POSITIONS)
    slot_pos = jnp.repeat(slot_table % PROMPT_BLOCKS * BLOCK_POSITIONS, BLOCK_POSITIONS) + jnp.tile(
        jnp.arange(BLOCK_POSITIONS, dtype=jnp.int32), slots_here
    )
    visible = (tenant_beam[:, None] == slot_tenant[None, :]) & (
        slot_pos[None, :] < length_beam[:, None]
    )
    prompt_mask = visible[None, :, None, :]
    keys_flat = prompt_key_slots.transpose(1, 0, 2, 3).reshape(heads_kv, keys_here, HEAD_WIDTH)
    values_flat = prompt_value_slots.transpose(1, 0, 2, 3).reshape(heads_kv, keys_here, HEAD_WIDTH)
    local_beam = jnp.arange(own_rows, dtype=jnp.int32)
    base_rows = local_beam // REQUEST_BEAMS * REQUEST_BEAMS
    trailing_zeros = jnp.zeros((own_rows, heads_kv, DECODE_STEPS, HEAD_WIDTH), jnp.bfloat16)
    cached_key_rows = jnp.concatenate([generated_keys, trailing_zeros], axis=2)
    cached_value_rows = jnp.concatenate([generated_values, trailing_zeros], axis=2)
    gen_pos = jnp.arange(EARLIER_TOKENS + DECODE_STEPS, dtype=jnp.int32)
    w_both = jnp.concatenate([w_gate, w_up], axis=1)
    residual = embeds[0].astype(jnp.float32)
    squares = jnp.sum(residual * residual, axis=1)
    normed = (residual * attn_norm).astype(jnp.bfloat16)
    partial_value = jnp.dot(normed, query_key_value_weight, preferred_element_type=jnp.float32)
    own_value = scatter_sum_flat(
        jnp.concatenate([partial_value, squares[:, None]], axis=1), "blk"
    )
    inverse = lax.rsqrt(own_value[:, -1] / MODEL_WIDTH + 1e-05)
    own_proj = (own_value[:, :-1] * inverse[:, None]).reshape(own_rows, heads_kv, col_width, HEAD_WIDTH)
    own_length = lax.dynamic_slice_in_dim(length_beam, my_index * own_rows, own_rows, 0)
    own_angle = angles_for(own_length + EARLIER_TOKENS + 0, HEAD_WIDTH)
    own_queries = rotate(own_proj[:, :, :group_queries], own_angle[:, None, None, :]).astype(
        jnp.bfloat16
    )
    query_rows = gather_rows(own_queries, "blk")
    new_key = rotate(own_proj[:, :, group_queries], own_angle[:, None, :]).astype(jnp.bfloat16)
    new_value = own_proj[:, :, group_queries + 1].astype(jnp.bfloat16)
    parent_rows = base_rows + parents[0]
    cached_key_rows = (
        jnp.take(cached_key_rows, parent_rows, axis=0).at[:, :, EARLIER_TOKENS].set(new_key)
    )
    cached_value_rows = (
        jnp.take(cached_value_rows, parent_rows, axis=0).at[:, :, EARLIER_TOKENS].set(new_value)
    )
    grouped = query_rows.transpose(1, 0, 2, 3).reshape(
        heads_kv, all_rows * group_queries, HEAD_WIDTH
    )
    scores = jnp.einsum("kqd,knd->kqn", grouped, keys_flat, preferred_element_type=jnp.float32)
    scores = scores.reshape(heads_kv, all_rows, group_queries, keys_here) * score_scale
    top_score = jnp.max(jnp.where(prompt_mask, scores, masked_score), axis=3)
    weights = jnp.where(prompt_mask, jnp.exp(scores - top_score[..., None]), 0.0)
    total_mass = jnp.sum(weights, axis=3)
    flat_weights = weights.reshape(heads_kv, all_rows * group_queries, keys_here).astype(
        jnp.bfloat16
    )
    summed = jnp.einsum(
        "kqn,knd->kqd", flat_weights, values_flat, preferred_element_type=jnp.float32
    )
    summed = summed.reshape(heads_kv, all_rows, group_queries, HEAD_WIDTH)
    packed = jnp.concatenate([summed, top_score[..., None], total_mass[..., None]], axis=3)
    packed = packed.transpose(1, 0, 2, 3).reshape(blocks, -1)
    parts = lax.all_to_all(packed, "blk", 0, 0, tiled=False).reshape(
        blocks, own_rows, heads_kv, group_queries, HEAD_WIDTH + 2
    )
    part_top = parts[..., HEAD_WIDTH]
    prompt_top = jnp.max(part_top, axis=0)
    part_factor = jnp.exp(part_top - prompt_top[None])
    prompt_mass = jnp.sum(parts[..., HEAD_WIDTH + 1] * part_factor, axis=0)
    prompt_sum = jnp.sum(parts[..., :HEAD_WIDTH] * part_factor[..., None], axis=0)
    prompt_top = prompt_top.transpose(1, 0, 2)
    prompt_mass = prompt_mass.transpose(1, 0, 2)
    prompt_sum = prompt_sum.transpose(1, 0, 2, 3)
    gen_scores = (
        jnp.einsum(
            "bkgd,bknd->kbgn", own_queries, cached_key_rows, preferred_element_type=jnp.float32
        )
        * score_scale
    )
    live = (gen_pos <= EARLIER_TOKENS)[None, None, None, :]
    gen_top = jnp.max(jnp.where(live, gen_scores, masked_score), axis=3)
    best = jnp.maximum(prompt_top, gen_top)
    gen_weights = jnp.where(live, jnp.exp(gen_scores - best[..., None]), 0.0)
    shift = jnp.exp(prompt_top - best)
    full_mass = prompt_mass * shift + jnp.sum(gen_weights, axis=3)
    gen_sum = jnp.einsum(
        "kbgn,bknd->kbgd",
        gen_weights.astype(jnp.bfloat16),
        cached_value_rows,
        preferred_element_type=jnp.float32,
    )
    attended_output = (prompt_sum * shift[..., None] + gen_sum) / full_mass[..., None]
    heads_out = (
        attended_output.transpose(1, 0, 2, 3)
        .reshape(own_rows, heads_kv * group_queries * HEAD_WIDTH)
        .astype(jnp.bfloat16)
    )
    head_part = jnp.dot(
        gather_rows(heads_out, "blk"),
        w_out,
        preferred_element_type=jnp.float32,
    )
    after_attn = residual + across_heads(head_part)
    squares2 = jnp.sum(after_attn * after_attn, axis=1)
    normed2 = (after_attn * mlp_norm).astype(jnp.bfloat16)
    squares2_high = squares2.astype(jnp.bfloat16)
    squares2_low = (squares2 - squares2_high.astype(jnp.float32)).astype(jnp.bfloat16)
    mixed = scatter_sum(
        jnp.concatenate(
            [
                jnp.dot(normed2, w_both, preferred_element_type=jnp.float32).astype(jnp.bfloat16),
                squares2_high[:, None],
                squares2_low[:, None],
            ],
            axis=1,
        ),
        "blk",
        jnp.float32,
    )
    own_inverse = lax.rsqrt((mixed[:, -2] + mixed[:, -1]) / MODEL_WIDTH + 1e-05)
    gate = mixed[:, :unit_count] * own_inverse[:, None]
    upper = mixed[:, unit_count : 2 * unit_count] * own_inverse[:, None]
    hidden = (jax.nn.silu(gate) * upper).astype(jnp.bfloat16)
    ff_part = jnp.dot(
        gather_rows(hidden, "blk"),
        w_down,
        preferred_element_type=jnp.float32,
    )
    outputs = [after_attn + across_heads(ff_part)]
    return (jnp.stack(outputs), cached_key_rows, cached_value_rows)


def solution(mesh):
    in_specs = (
        P(None, None, "blk"),
        P("blk"),
        P("blk", "kv"),
        P("kv", "blk"),
        P("blk"),
        P("blk", "kv"),
        P("blk", "kv"),
        P("kv", "blk"),
        P("blk", "kv", None, None),
        P("blk", "kv", None, None),
        P("blk", "kv", None, None),
        P("blk", "kv", None, None),
        P(None, "blk"),
        P(),
        P(),
        P("blk"),
    )
    out_specs = (P(None, None, "blk"), P("blk", "kv", None, None), P("blk", "kv", None, None))
    return jax.shard_map(body, mesh=mesh, in_specs=in_specs, out_specs=out_specs, check_vma=False)
```
